128 devices in a mesh: space: 8 (over z, core), vel: 16 (over x, y).
Axes of the slice: x: 4, y: 4, z: 4, core: 2. Of those that a mesh axis runs over, the one named last changes fastest.
Arguments:
- dist: bfloat16 [7168, 16, 16, 128], P('vel', 'space'), may hold values from 0.25 to 4
- vel_map: int32 [7168], P('vel'), may hold values from 0 to 13823, as said below
- cell_mask: int32 [16, 16, 128], P('space'), may hold values from 0 to 2, as said below
- w_modes: bfloat16 [512, 7168], replicated, may hold values from -0.0625 to 0.0625
- e_modes: bfloat16 [7168, 512], replicated, may hold values from -0.25 to 0.25
- rates: float32 [512], replicated, may hold values from 0.1 to 1
Outputs:
- dist_out: bfloat16 [7168, 16, 16, 128], P('vel', 'space')
The draws below stay inside these ranges and needn't reach their ends.
Inputs may be any that keep to these rules, and one draw needn't show every extreme that they name: `vel_map`: distinct lattice indices: the 7168 points of the 24^3 cube nearest its centre, in a random order. `cell_mask`: cells with x index 0 are fluid.
All inputs are finite; a program needn't handle non-finite values.
Results may differ from the reference program's by a relative error of at most 0.0054.
Values may be sent and summed in bfloat16 or wider, within the bound.
No kernel may reach another device: no remote copies, remote signals or barrier semaphores. Data moves between devices by JAX's collectives and lax.ppermute only.
A program may use at most 192 MiB of HBM per device.

```python
import math
import jax
import jax.numpy as jnp
from jax import lax

V = 7168
VGRID = 24
K = 512
NX = 128
NY = 16
STEPS = 2
NZ = 16
NSLAB = 8
CELLS = 4096


def draw_vel_map(key, part):
    side = VGRID
    total = side * side * side
    index = jnp.arange(total, dtype=jnp.int32)
    first = index // (side * side)
    second = index // side % side
    third = index % side
    radius = (2 * first - (side - 1)) ** 2 + (2 * second - (side - 1)) ** 2 + (2 * third - (side - 1)) ** 2
    tiebreak = jax.random.permutation(jax.random.fold_in(key, 3), total).astype(jnp.int32)
    score = -(radius * total + tiebreak)
    picked = lax.top_k(score, V)[1].astype(jnp.int32)
    chosen = jnp.take(index, picked)
    return jax.random.permutation(jax.random.fold_in(key, 5), chosen).astype(jnp.int32)


def draw_cell_mask(key, part):
    level = jax.random.randint(jax.random.fold_in(key, 11), (NZ, NY, NX), 0, 5).astype(jnp.int32)
    marks = jnp.where(level < 3, 0, level - 2).astype(jnp.int32)
    column = jnp.arange(NX, dtype=jnp.int32)[None, None, :]
    return jnp.where(column == 0, 0, marks).astype(jnp.int32)


def level_of(rng, shape, split, smallest, high):
    loudness = 1.0
    for axis_at, parts in split:
        draws = jax.random.uniform(jax.random.fold_in(jax.random.fold_in(rng, 6), axis_at), (parts,), jnp.float32, smallest / len(split), high / len(split))
        loudness = loudness * jnp.repeat(jnp.exp(draws), shape[axis_at] // parts).reshape((-1,) + (1,) * (len(shape) - 1 - axis_at))
    return loudness


def scatter_about(key, dims, deviation, reach, kind=jnp.bfloat16):
    result = jax.random.normal(key, dims, jnp.float32) * deviation
    return jnp.minimum(jnp.maximum(result, -reach), reach).astype(kind)


def setup_inputs(seed: int = 0) -> dict:
    keys = jax.random.split(jax.random.key(seed), 7)
    dist = jnp.clip(jnp.exp(math.log(4.0) - 2.7725887 * jax.random.uniform(keys[0], (V, NZ, NY, NX), jnp.float32) ** level_of(keys[0], (V, NZ, NY, NX), ((0, 16), (1, 8)), -0.2, 0.2)), 0.25, 4.0).astype(jnp.bfloat16)
    vel_map = draw_vel_map(jax.random.fold_in(keys[6], 71), 0)
    cell_mask = draw_cell_mask(jax.random.fold_in(keys[6], 71), 0)
    w_modes = scatter_about(keys[3], (K, V), V ** -0.5, 0.0625)
    e_modes = scatter_about(keys[4], (V, K), K ** -0.5, 0.25)
    rates = jnp.clip(jnp.exp(jax.random.uniform(keys[5], (K,), jnp.float32, math.log(0.1), math.log(1.0))), 0.1, 1.0)
    return dict(dist=dist, vel_map=vel_map, cell_mask=cell_mask, w_modes=w_modes, e_modes=e_modes, rates=rates)


def components(vel_map):
    side = VGRID
    first = (vel_map // (side * side)).astype(jnp.float32)
    second = ((vel_map // side) % side).astype(jnp.float32)
    third = (vel_map % side).astype(jnp.float32)
    centre = (side - 1) / 2.0
    half_side = side / 2.0
    return (0.3 * (first - centre) / half_side, 0.3 * (second - centre) / half_side, 0.3 * (third - centre) / half_side)


def transport_block(call_arguments):
    block, cx_blk, cy_blk, cz_blk, tmask = call_arguments
    whole = jnp.pad(block.astype(jnp.float32), ((0, 0), (1, 1), (1, 1), (1, 1)))
    center = whole[:, 1:-1, 1:-1, 1:-1]
    ax = cx_blk[:, None, None, None]
    ay = cy_blk[:, None, None, None]
    az = cz_blk[:, None, None, None]
    flux = jnp.maximum(ax, 0.0) * (center - whole[:, 1:-1, 1:-1, :-2]) + jnp.minimum(ax, 0.0) * (whole[:, 1:-1, 1:-1, 2:] - center)
    flux = flux + jnp.maximum(ay, 0.0) * (center - whole[:, 1:-1, :-2, 1:-1]) + jnp.minimum(ay, 0.0) * (whole[:, 1:-1, 2:, 1:-1] - center)
    flux = flux + jnp.maximum(az, 0.0) * (center - whole[:, :-2, 1:-1, 1:-1]) + jnp.minimum(az, 0.0) * (whole[:, 2:, 1:-1, 1:-1] - center)
    return (center - tmask[None] * flux).astype(jnp.bfloat16)


def reference(dist, vel_map, cell_mask, w_modes, e_modes, rates):
    ax, ay, az = components(vel_map)
    tmask = (cell_mask != 1).astype(jnp.float32)
    cmask = jnp.where(cell_mask == 0, 1.0, jnp.where(cell_mask == 2, 0.5, 0.0)).astype(jnp.float32)
    blocks = V // 64
    f = dist
    for step in range(STEPS):
        def one_block(call_arguments):
            return transport_block((call_arguments[0], call_arguments[1], call_arguments[2], call_arguments[3], tmask))
        half = lax.map(one_block, (f.reshape(blocks, 64, NZ, NY, NX), ax.reshape(blocks, 64), ay.reshape(blocks, 64), az.reshape(blocks, 64)))
        half = half.reshape(V, NSLAB, CELLS).transpose(1, 0, 2)

        def collide(call_arguments):
            spatial_layer, collision_term = call_arguments
            moments = jnp.dot(w_modes, spatial_layer, preferred_element_type=jnp.float32)
            delta = (rates[:, None] * moments).astype(jnp.bfloat16)
            modal_adjustment = jnp.dot(e_modes, delta, preferred_element_type=jnp.float32)
            return (spatial_layer.astype(jnp.float32) - collision_term[None, :] * modal_adjustment).astype(jnp.bfloat16)

        new = lax.map(collide, (half, cmask.reshape(NSLAB, CELLS)))
        f = new.transpose(1, 0, 2).reshape(V, NZ, NY, NX)
    return f
```

```python
import functools

import jax
import jax.numpy as jnp
from jax import lax
from jax.experimental import pallas as pl
from jax.experimental.pallas import tpu as pltpu
from jax.sharding import PartitionSpec as P

VGRID = 24
STEPS = 2
VBLOCK = 64


def components(vel_map):
    side = VGRID
    first = (vel_map // (side * side)).astype(jnp.float32)
    second = (vel_map // side % side).astype(jnp.float32)
    third = (vel_map % side).astype(jnp.float32)
    centre = (side - 1) / 2.0
    half_side = side / 2.0
    return (
        0.3 * (first - centre) / half_side,
        0.3 * (second - centre) / half_side,
        0.3 * (third - centre) / half_side,
    )


def transport_kernel(ny, f_ref, lo_ref, hi_ref, coef_ref, tm_ref, out_ref):
    rows, tv, nx = f_ref.shape
    nzl = rows // ny
    ax = coef_ref[0]
    ay = coef_ref[1]
    az = coef_ref[2]
    zero = jnp.zeros((tv, nx), jnp.float32)
    px, mx = jnp.maximum(ax, 0.0), jnp.minimum(ax, 0.0)
    py, my = jnp.maximum(ay, 0.0), jnp.minimum(ay, 0.0)
    pz, mz = jnp.maximum(az, 0.0), jnp.minimum(az, 0.0)
    lane = lax.broadcasted_iota(jnp.int32, (tv, nx), 1)

    def load(ref, i):
        return ref[i].astype(jnp.float32)

    for w in range(rows):
        z, y = divmod(w, ny)
        c = load(f_ref, w)
        x_low = jnp.where(lane == 0, 0.0, pltpu.roll(c, 1, 1))
        x_high = jnp.where(lane == nx - 1, 0.0, pltpu.roll(c, nx - 1, 1))
        y_low = load(f_ref, w - 1) if y > 0 else zero
        y_high = load(f_ref, w + 1) if y < ny - 1 else zero
        z_low = load(f_ref, w - ny) if z > 0 else load(lo_ref, y)
        z_high = load(f_ref, w + ny) if z < nzl - 1 else load(hi_ref, y)
        flux = px * (c - x_low) + mx * (x_high - c)
        flux = flux + py * (c - y_low) + my * (y_high - c)
        flux = flux + pz * (c - z_low) + mz * (z_high - c)
        out_ref[w] = (c - tm_ref[w : w + 1, :] * flux).astype(out_ref.dtype)


def transport(f, lo, hi, coef, tm, ny):
    rows, vb, nx = f.shape
    tv = VBLOCK
    return pl.pallas_call(
        functools.partial(transport_kernel, ny),
        out_shape=jax.ShapeDtypeStruct(f.shape, f.dtype),
        grid=(vb // tv,),
        in_specs=[
            pl.BlockSpec((rows, tv, nx), lambda i: (0, i, 0)),
            pl.BlockSpec((ny, tv, nx), lambda i: (0, i, 0)),
            pl.BlockSpec((ny, tv, nx), lambda i: (0, i, 0)),
            pl.BlockSpec((3, tv, nx), lambda i: (0, i, 0)),
            pl.BlockSpec((rows, nx), lambda i: (0, 0)),
        ],
        out_specs=pl.BlockSpec((rows, tv, nx), lambda i: (0, i, 0)),
        cost_estimate=pl.CostEstimate(
            flops=30 * rows * vb * nx, transcendentals=0, bytes_accessed=4 * rows * vb * nx
        ),
    )(f, lo, hi, coef, tm)


def per_device(dist, vel_map, cell_mask, w_modes, e_modes, rates):
    vb, nzl, ny, nx = dist.shape
    rows = nzl * ny
    groups = lax.axis_size("vel")
    spaces = lax.axis_size("space")
    chunk = rows // groups
    kmodes = w_modes.shape[0]
    comp_x, comp_y, comp_z = components(vel_map)
    coef = jnp.broadcast_to(jnp.stack([comp_x, comp_y, comp_z])[:, :, None], (3, vb, nx))
    tm = (cell_mask != 1).astype(jnp.float32).reshape(rows, nx)
    cmask = jnp.where(cell_mask == 0, 1.0, jnp.where(cell_mask == 2, 0.5, 0.0)).astype(jnp.float32)
    cm = lax.dynamic_slice_in_dim(cmask.reshape(rows, nx), lax.axis_index("vel") * chunk, chunk, 0)
    w3 = w_modes.reshape(kmodes, groups, vb)
    e3 = e_modes.reshape(groups, vb, kmodes)
    up = [(i, i + 1) for i in range(spaces - 1)]
    down = [(i + 1, i) for i in range(spaces - 1)]

    f = jnp.transpose(dist, (1, 2, 0, 3)).reshape(rows, vb, nx)
    for step in range(STEPS):
        lo = lax.ppermute(f[rows - ny :], "space", up)
        hi = lax.ppermute(f[:ny], "space", down)
        half = transport(f, lo, hi, coef, tm, ny)
        send = half.reshape(groups, chunk, vb, nx)
        recv = lax.all_to_all(send, "vel", 0, 0, tiled=True)
        moments = jnp.einsum("ksv,srvx->krx", w3, recv, preferred_element_type=jnp.float32)
        delta = (rates[:, None, None] * moments).astype(jnp.bfloat16)
        adjustment = jnp.einsum("svk,krx->srvx", e3, delta, preferred_element_type=jnp.float32)
        post = (recv.astype(jnp.float32) - cm[None, :, None, :] * adjustment).astype(jnp.bfloat16)
        back = lax.all_to_all(post, "vel", 0, 0, tiled=True)
        f = back.reshape(rows, vb, nx)
    return jnp.transpose(f.reshape(nzl, ny, vb, nx), (2, 0, 1, 3))


def solution(mesh):
    placed = (P("vel", "space", None, None), P("vel"), P("space", None, None), P(), P(), P())
    return jax.shard_map(
        per_device,
        mesh=mesh,
        in_specs=placed,
        out_specs=P("vel", "space", None, None),
        check_vma=False,
    )
```

```python
import functools

import jax
import jax.numpy as jnp
from jax import lax
from jax.experimental import pallas as pl
from jax.experimental.pallas import tpu as pltpu
from jax.sharding import PartitionSpec as P

VGRID = 24
STEPS = 2
VBLOCK = 64


def components(vel_map):
    side = VGRID
    first = (vel_map // (side * side)).astype(jnp.float32)
    second = (vel_map // side % side).astype(jnp.float32)
    third = (vel_map % side).astype(jnp.float32)
    centre = (side - 1) / 2.0
    half_side = side / 2.0
    return (
        0.3 * (first - centre) / half_side,
        0.3 * (second - centre) / half_side,
        0.3 * (third - centre) / half_side,
    )


def transport_kernel(ny, f_ref, lo_ref, hi_ref, coef_ref, tm_ref, out_ref):
    rows, tv, nx = f_ref.shape
    nzl = rows // ny
    ax = coef_ref[0]
    ay = coef_ref[1]
    az = coef_ref[2]
    zero = jnp.zeros((tv, nx), jnp.float32)
    px, mx = jnp.maximum(ax, 0.0), jnp.minimum(ax, 0.0)
    py, my = jnp.maximum(ay, 0.0), jnp.minimum(ay, 0.0)
    pz, mz = jnp.maximum(az, 0.0), jnp.minimum(az, 0.0)
    lane = lax.broadcasted_iota(jnp.int32, (tv, nx), 1)

    def load(ref, i):
        return ref[i].astype(jnp.float32)

    for w in range(rows):
        z, y = divmod(w, ny)
        c = load(f_ref, w)
        x_low = jnp.where(lane == 0, 0.0, pltpu.roll(c, 1, 1))
        x_high = jnp.where(lane == nx - 1, 0.0, pltpu.roll(c, nx - 1, 1))
        y_low = load(f_ref, w - 1) if y > 0 else zero
        y_high = load(f_ref, w + 1) if y < ny - 1 else zero
        z_low = load(f_ref, w - ny) if z > 0 else load(lo_ref, y)
        z_high = load(f_ref, w + ny) if z < nzl - 1 else load(hi_ref, y)
        flux = px * (c - x_low) + mx * (x_high - c)
        flux = flux + py * (c - y_low) + my * (y_high - c)
        flux = flux + pz * (c - z_low) + mz * (z_high - c)
        out_ref[w] = (c - tm_ref[w : w + 1, :] * flux).astype(out_ref.dtype)


def transport(f, lo, hi, coef, tm, ny):
    rows, vb, nx = f.shape
    tv = VBLOCK
    return pl.pallas_call(
        functools.partial(transport_kernel, ny),
        out_shape=jax.ShapeDtypeStruct(f.shape, f.dtype),
        grid=(vb // tv,),
        in_specs=[
            pl.BlockSpec((rows, tv, nx), lambda i: (0, i, 0)),
            pl.BlockSpec((ny, tv, nx), lambda i: (0, i, 0)),
            pl.BlockSpec((ny, tv, nx), lambda i: (0, i, 0)),
            pl.BlockSpec((3, tv, nx), lambda i: (0, i, 0)),
            pl.BlockSpec((rows, nx), lambda i: (0, 0)),
        ],
        out_specs=pl.BlockSpec((rows, tv, nx), lambda i: (0, i, 0)),
        cost_estimate=pl.CostEstimate(
            flops=30 * rows * vb * nx, transcendentals=0, bytes_accessed=4 * rows * vb * nx
        ),
    )(f, lo, hi, coef, tm)


def per_device(dist, vel_map, cell_mask, w_modes, e_modes, rates):
    vb, nzl, ny, nx = dist.shape
    rows = nzl * ny
    groups = lax.axis_size("vel")
    spaces = lax.axis_size("space")
    chunk = rows // groups
    kmodes = w_modes.shape[0]
    comp_x, comp_y, comp_z = components(vel_map)
    coef = jnp.broadcast_to(jnp.stack([comp_x, comp_y, comp_z])[:, :, None], (3, vb, nx))
    tm = (cell_mask != 1).astype(jnp.float32).reshape(rows, nx)
    cmask = jnp.where(cell_mask == 0, 1.0, jnp.where(cell_mask == 2, 0.5, 0.0)).astype(jnp.float32)
    cm_all = cmask.reshape(rows, nx)
    w3 = w_modes.reshape(kmodes, groups, vb)
    e_local = lax.dynamic_slice_in_dim(e_modes, lax.axis_index("vel") * vb, vb, 0)
    up = [(i, i + 1) for i in range(spaces - 1)]
    down = [(i + 1, i) for i in range(spaces - 1)]

    f = jnp.transpose(dist, (1, 2, 0, 3)).reshape(rows, vb, nx)
    for step in range(STEPS):
        lo = lax.ppermute(f[rows - ny :], "space", up)
        hi = lax.ppermute(f[:ny], "space", down)
        half = transport(f, lo, hi, coef, tm, ny)
        send = half.reshape(groups, chunk, vb, nx)
        recv = lax.all_to_all(send, "vel", 0, 0, tiled=True)
        moments = jnp.einsum("ksv,srvx->krx", w3, recv, preferred_element_type=jnp.float32)
        delta = (rates[:, None, None] * moments).astype(jnp.bfloat16)
        delta_all = lax.all_gather(delta, "vel", axis=1, tiled=True)
        adjustment = jnp.einsum("vk,kwx->wvx", e_local, delta_all, preferred_element_type=jnp.float32)
        f = (half.astype(jnp.float32) - cm_all[:, None, :] * adjustment).astype(jnp.bfloat16)
    return jnp.transpose(f.reshape(nzl, ny, vb, nx), (2, 0, 1, 3))


def solution(mesh):
    placed = (P("vel", "space", None, None), P("vel"), P("space", None, None), P(), P(), P())
    return jax.shard_map(
        per_device,
        mesh=mesh,
        in_specs=placed,
        out_specs=P("vel", "space", None, None),
        check_vma=False,
    )
```

```python
import functools

import jax
import jax.numpy as jnp
from jax import lax
from jax.experimental import pallas as pl
from jax.experimental.pallas import tpu as pltpu
from jax.sharding import PartitionSpec as P

VGRID = 24
STEPS = 2
VBLOCK = 32
PARTS = 2


def components(vel_map):
    side = VGRID
    first = (vel_map // (side * side)).astype(jnp.float32)
    second = (vel_map // side % side).astype(jnp.float32)
    third = (vel_map % side).astype(jnp.float32)
    centre = (side - 1) / 2.0
    half_side = side / 2.0
    return (
        0.3 * (first - centre) / half_side,
        0.3 * (second - centre) / half_side,
        0.3 * (third - centre) / half_side,
    )


def transport_kernel(ny, f_ref, lo_ref, hi_ref, coef_ref, tm_ref, out_ref):
    rows, tv, nx = f_ref.shape
    nzl = rows // ny
    ax = coef_ref[0]
    ay = coef_ref[1]
    az = coef_ref[2]
    zero = jnp.zeros((tv, nx), jnp.float32)
    px, mx = jnp.maximum(ax, 0.0), jnp.minimum(ax, 0.0)
    py, my = jnp.maximum(ay, 0.0), jnp.minimum(ay, 0.0)
    pz, mz = jnp.maximum(az, 0.0), jnp.minimum(az, 0.0)
    lane = lax.broadcasted_iota(jnp.int32, (tv, nx), 1)

    def load(ref, i):
        return ref[i].astype(jnp.float32)

    for w in range(rows):
        z, y = divmod(w, ny)
        c = load(f_ref, w)
        x_low = jnp.where(lane == 0, 0.0, pltpu.roll(c, 1, 1))
        x_high = jnp.where(lane == nx - 1, 0.0, pltpu.roll(c, nx - 1, 1))
        y_low = load(f_ref, w - 1) if y > 0 else zero
        y_high = load(f_ref, w + 1) if y < ny - 1 else zero
        z_low = load(f_ref, w - ny) if z > 0 else load(lo_ref, y)
        z_high = load(f_ref, w + ny) if z < nzl - 1 else load(hi_ref, y)
        flux = px * (c - x_low) + mx * (x_high - c)
        flux = flux + py * (c - y_low) + my * (y_high - c)
        flux = flux + pz * (c - z_low) + mz * (z_high - c)
        out_ref[w] = (c - tm_ref[w : w + 1, :] * flux).astype(out_ref.dtype)


def transport(f, lo, hi, coef, tm, ny):
    rows, vb, nx = f.shape
    tv = VBLOCK
    return pl.pallas_call(
        functools.partial(transport_kernel, ny),
        out_shape=jax.ShapeDtypeStruct(f.shape, f.dtype),
        grid=(vb // tv,),
        in_specs=[
            pl.BlockSpec((rows, tv, nx), lambda i: (0, i, 0)),
            pl.BlockSpec((ny, tv, nx), lambda i: (0, i, 0)),
            pl.BlockSpec((ny, tv, nx), lambda i: (0, i, 0)),
            pl.BlockSpec((3, tv, nx), lambda i: (0, i, 0)),
            pl.BlockSpec((rows, nx), lambda i: (0, 0)),
        ],
        out_specs=pl.BlockSpec((rows, tv, nx), lambda i: (0, i, 0)),
        cost_estimate=pl.CostEstimate(
            flops=30 * rows * vb * nx, transcendentals=0, bytes_accessed=4 * rows * vb * nx
        ),
    )(f, lo, hi, coef, tm)


def per_device(dist, vel_map, cell_mask, w_modes, e_modes, rates):
    vb, nzl, ny, nx = dist.shape
    rows = nzl * ny
    groups = lax.axis_size("vel")
    spaces = lax.axis_size("space")
    chunk = rows // groups
    kmodes = w_modes.shape[0]
    part = vb // PARTS
    comp_x, comp_y, comp_z = components(vel_map)
    coef = jnp.broadcast_to(jnp.stack([comp_x, comp_y, comp_z])[:, :, None], (3, vb, nx))
    tm = (cell_mask != 1).astype(jnp.float32).reshape(rows, nx)
    cmask = jnp.where(cell_mask == 0, 1.0, jnp.where(cell_mask == 2, 0.5, 0.0)).astype(jnp.float32)
    cm = lax.dynamic_slice_in_dim(cmask.reshape(rows, nx), lax.axis_index("vel") * chunk, chunk, 0)
    w3 = w_modes.reshape(kmodes, groups, vb)
    e3 = e_modes.reshape(groups, vb, kmodes)
    up = [(i, i + 1) for i in range(spaces - 1)]
    down = [(i + 1, i) for i in range(spaces - 1)]
    pieces = [slice(h * part, (h + 1) * part) for h in range(PARTS)]

    whole = jnp.transpose(dist, (1, 2, 0, 3)).reshape(rows, vb, nx)
    fs = [whole[:, p] for p in pieces]
    for step in range(STEPS):
        recvs = []
        for h, p in enumerate(pieces):
            f = fs[h]
            lo = lax.ppermute(f[rows - ny :], "space", up)
            hi = lax.ppermute(f[:ny], "space", down)
            half = transport(f, lo, hi, coef[:, p], tm, ny)
            recvs.append(lax.all_to_all(half.reshape(groups, chunk, part, nx), "vel", 0, 0, tiled=True))
        moments = None
        for h, p in enumerate(pieces):
            term = jnp.einsum("ksv,srvx->krx", w3[:, :, p], recvs[h], preferred_element_type=jnp.float32)
            moments = term if moments is None else moments + term
        delta = (rates[:, None, None] * moments).astype(jnp.bfloat16)
        fs = []
        for h, p in enumerate(pieces):
            adjustment = jnp.einsum("svk,krx->srvx", e3[:, p], delta, preferred_element_type=jnp.float32)
            post = (recvs[h].astype(jnp.float32) - cm[None, :, None, :] * adjustment).astype(jnp.bfloat16)
            fs.append(lax.all_to_all(post, "vel", 0, 0, tiled=True).reshape(rows, part, nx))
    whole = jnp.concatenate(fs, axis=1)
    return jnp.transpose(whole.reshape(nzl, ny, vb, nx), (2, 0, 1, 3))


def solution(mesh):
    placed = (P("vel", "space", None, None), P("vel"), P("space", None, None), P(), P(), P())
    return jax.shard_map(
        per_device,
        mesh=mesh,
        in_specs=placed,
        out_specs=P("vel", "space", None, None),
        check_vma=False,
    )
```

```python
import functools

import jax
import jax.numpy as jnp
from jax import lax
from jax.experimental import pallas as pl
from jax.experimental.pallas import tpu as pltpu
from jax.sharding import PartitionSpec as P

VGRID = 24
STEPS = 2
VBLOCK = 112
PARTS = 2


def components(vel_map):
    side = VGRID
    first = (vel_map // (side * side)).astype(jnp.float32)
    second = (vel_map // side % side).astype(jnp.float32)
    third = (vel_map % side).astype(jnp.float32)
    centre = (side - 1) / 2.0
    half_side = side / 2.0
    return (
        0.3 * (first - centre) / half_side,
        0.3 * (second - centre) / half_side,
        0.3 * (third - centre) / half_side,
    )


def transport_kernel(ny, f_ref, lo_ref, hi_ref, coef_ref, tm_ref, out_ref, ext_ref):
    rows, tv, nx = f_ref.shape
    ext_ref[pl.ds(0, ny)] = lo_ref[...].astype(jnp.float32)
    ext_ref[pl.ds(ny, rows)] = f_ref[...].astype(jnp.float32)
    ext_ref[pl.ds(ny + rows, ny)] = hi_ref[...].astype(jnp.float32)
    ax = coef_ref[0]
    ay = coef_ref[1]
    az = coef_ref[2]
    gx, gy, gz = ax > 0.0, ay > 0.0, az > 0.0
    wx, wy, wz = jnp.abs(ax), jnp.abs(ay), jnp.abs(az)
    lane = lax.broadcasted_iota(jnp.int32, (tv, nx), 1)
    edge_x = (gx & (lane == 0)) | (jnp.logical_not(gx) & (lane == nx - 1))
    zero = jnp.zeros((tv, nx), jnp.float32)

    for w in range(rows):
        y = w % ny
        e = w + ny
        c = ext_ref[e]
        n_x = jnp.where(edge_x, 0.0, jnp.where(gx, pltpu.roll(c, 1, 1), pltpu.roll(c, nx - 1, 1)))
        y_low = ext_ref[e - 1] if y > 0 else zero
        y_high = ext_ref[e + 1] if y < ny - 1 else zero
        n_y = jnp.where(gy, y_low, y_high)
        n_z = jnp.where(gz, ext_ref[e - ny], ext_ref[e + ny])
        flux = wx * (c - n_x) + wy * (c - n_y)
        flux = flux + wz * (c - n_z)
        out_ref[w] = (c - tm_ref[w : w + 1, :] * flux).astype(out_ref.dtype)


def transport(f, lo, hi, coef, tm, ny):
    rows, vb, nx = f.shape
    tv = min(VBLOCK, vb)
    return pl.pallas_call(
        functools.partial(transport_kernel, ny),
        out_shape=jax.ShapeDtypeStruct(f.shape, f.dtype),
        grid=(vb // tv,),
        in_specs=[
            pl.BlockSpec((rows, tv, nx), lambda i: (0, i, 0)),
            pl.BlockSpec((ny, tv, nx), lambda i: (0, i, 0)),
            pl.BlockSpec((ny, tv, nx), lambda i: (0, i, 0)),
            pl.BlockSpec((3, tv, nx), lambda i: (0, i, 0)),
            pl.BlockSpec((rows, nx), lambda i: (0, 0)),
        ],
        out_specs=pl.BlockSpec((rows, tv, nx), lambda i: (0, i, 0)),
        scratch_shapes=[pltpu.VMEM((rows + 2 * ny, tv, nx), jnp.float32)],
        cost_estimate=pl.CostEstimate(
            flops=20 * rows * vb * nx, transcendentals=0, bytes_accessed=4 * rows * vb * nx
        ),
    )(f, lo, hi, coef, tm)


def per_device(dist, vel_map, cell_mask, w_modes, e_modes, rates):
    vb, nzl, ny, nx = dist.shape
    rows = nzl * ny
    groups = lax.axis_size("vel")
    spaces = lax.axis_size("space")
    chunk = rows // groups
    kmodes = w_modes.shape[0]
    part = vb // PARTS
    comp_x, comp_y, comp_z = components(vel_map)
    coef = jnp.broadcast_to(jnp.stack([comp_x, comp_y, comp_z])[:, :, None], (3, vb, nx))
    tm = (cell_mask != 1).astype(jnp.float32).reshape(rows, nx)
    cmask = jnp.where(cell_mask == 0, 1.0, jnp.where(cell_mask == 2, 0.5, 0.0)).astype(jnp.float32)
    cm = lax.dynamic_slice_in_dim(cmask.reshape(rows, nx), lax.axis_index("vel") * chunk, chunk, 0)
    w3 = w_modes.reshape(kmodes, groups, vb)
    e3 = e_modes.reshape(groups, vb, kmodes)
    up = [(i, i + 1) for i in range(spaces - 1)]
    down = [(i + 1, i) for i in range(spaces - 1)]
    pieces = [slice(h * part, (h + 1) * part) for h in range(PARTS)]

    whole = jnp.transpose(dist, (1, 2, 0, 3)).reshape(rows, vb, nx)
    fs = [whole[:, p] for p in pieces]
    for step in range(STEPS):
        recvs = []
        for h, p in enumerate(pieces):
            f = fs[h]
            lo = lax.ppermute(f[rows - ny :], "space", up)
            hi = lax.ppermute(f[:ny], "space", down)
            half = transport(f, lo, hi, coef[:, p], tm, ny)
            recvs.append(lax.all_to_all(half.reshape(groups, chunk, part, nx), "vel", 0, 0, tiled=True))
        moments = None
        for h, p in enumerate(pieces):
            term = jnp.einsum("ksv,srvx->krx", w3[:, :, p], recvs[h], preferred_element_type=jnp.float32)
            moments = term if moments is None else moments + term
        delta = (rates[:, None, None] * moments).astype(jnp.bfloat16)
        fs = []
        for h, p in enumerate(pieces):
            adjustment = jnp.einsum("svk,krx->srvx", e3[:, p], delta, preferred_element_type=jnp.float32)
            post = (recvs[h].astype(jnp.float32) - cm[None, :, None, :] * adjustment).astype(jnp.bfloat16)
            fs.append(lax.all_to_all(post, "vel", 0, 0, tiled=True).reshape(rows, part, nx))
    whole = jnp.concatenate(fs, axis=1)
    return jnp.transpose(whole.reshape(nzl, ny, vb, nx), (2, 0, 1, 3))


def solution(mesh):
    placed = (P("vel", "space", None, None), P("vel"), P("space", None, None), P(), P(), P())
    return jax.shard_map(
        per_device,
        mesh=mesh,
        in_specs=placed,
        out_specs=P("vel", "space", None, None),
        check_vma=False,
    )
```

```python
import functools

import jax
import jax.numpy as jnp
from jax import lax
from jax.experimental import pallas as pl
from jax.experimental.pallas import tpu as pltpu
from jax.sharding import PartitionSpec as P

VGRID = 24
STEPS = 2
VBLOCK = 112
PARTS = 2


def components(vel_map):
    side = VGRID
    first = (vel_map // (side * side)).astype(jnp.float32)
    second = (vel_map // side % side).astype(jnp.float32)
    third = (vel_map % side).astype(jnp.float32)
    centre = (side - 1) / 2.0
    half_side = side / 2.0
    return (
        0.3 * (first - centre) / half_side,
        0.3 * (second - centre) / half_side,
        0.3 * (third - centre) / half_side,
    )


def transport_kernel(ny, f_ref, lo_ref, hi_ref, coef_ref, tm_ref, out_ref, ext_ref):
    rows, tv, nx = f_ref.shape
    ext_ref[pl.ds(0, ny)] = lo_ref[...].astype(jnp.float32)
    ext_ref[pl.ds(ny, rows)] = f_ref[...].astype(jnp.float32)
    ext_ref[pl.ds(ny + rows, ny)] = hi_ref[...].astype(jnp.float32)
    ax = coef_ref[0]
    ay = coef_ref[1]
    az = coef_ref[2]
    gx, gy, gz = ax > 0.0, ay > 0.0, az > 0.0
    wx, wy, wz = jnp.abs(ax), jnp.abs(ay), jnp.abs(az)
    lane = lax.broadcasted_iota(jnp.int32, (tv, nx), 1)
    edge_x = (gx & (lane == 0)) | (jnp.logical_not(gx) & (lane == nx - 1))
    zero = jnp.zeros((tv, nx), jnp.float32)

    for w in range(rows):
        y = w % ny
        e = w + ny
        c = ext_ref[e]
        n_x = jnp.where(edge_x, 0.0, jnp.where(gx, pltpu.roll(c, 1, 1), pltpu.roll(c, nx - 1, 1)))
        y_low = ext_ref[e - 1] if y > 0 else zero
        y_high = ext_ref[e + 1] if y < ny - 1 else zero
        n_y = jnp.where(gy, y_low, y_high)
        n_z = jnp.where(gz, ext_ref[e - ny], ext_ref[e + ny])
        flux = wx * (c - n_x) + wy * (c - n_y)
        flux = flux + wz * (c - n_z)
        out_ref[w] = (c - tm_ref[w : w + 1, :] * flux).astype(out_ref.dtype)


def transport(f, lo, hi, coef, tm, ny):
    rows, vb, nx = f.shape
    tv = min(VBLOCK, vb)
    return pl.pallas_call(
        functools.partial(transport_kernel, ny),
        out_shape=jax.ShapeDtypeStruct(f.shape, f.dtype),
        grid=(vb // tv,),
        in_specs=[
            pl.BlockSpec((rows, tv, nx), lambda i: (0, i, 0)),
            pl.BlockSpec((ny, tv, nx), lambda i: (0, i, 0)),
            pl.BlockSpec((ny, tv, nx), lambda i: (0, i, 0)),
            pl.BlockSpec((3, tv, nx), lambda i: (0, i, 0)),
            pl.BlockSpec((rows, nx), lambda i: (0, 0)),
        ],
        out_specs=pl.BlockSpec((rows, tv, nx), lambda i: (0, i, 0)),
        scratch_shapes=[pltpu.VMEM((rows + 2 * ny, tv, nx), jnp.float32)],
        cost_estimate=pl.CostEstimate(
            flops=20 * rows * vb * nx, transcendentals=0, bytes_accessed=4 * rows * vb * nx
        ),
    )(f, lo, hi, coef, tm)


def per_device(dist, vel_map, cell_mask, w_modes, e_modes, rates):
    vb, nzl, ny, nx = dist.shape
    rows = nzl * ny
    groups = lax.axis_size("vel")
    spaces = lax.axis_size("space")
    chunk = rows // groups
    kmodes = w_modes.shape[0]
    part = vb // PARTS
    comp_x, comp_y, comp_z = components(vel_map)
    coef = jnp.broadcast_to(jnp.stack([comp_x, comp_y, comp_z])[:, :, None], (3, vb, nx))
    tm = (cell_mask != 1).astype(jnp.float32).reshape(rows, nx)
    cmask = jnp.where(cell_mask == 0, 1.0, jnp.where(cell_mask == 2, 0.5, 0.0)).astype(jnp.float32)
    cm = lax.dynamic_slice_in_dim(cmask.reshape(rows, nx), lax.axis_index("vel") * chunk, chunk, 0)
    w3 = w_modes.reshape(kmodes, groups, vb)
    e3 = e_modes.reshape(groups, vb, kmodes)
    up = [(i, i + 1) for i in range(spaces - 1)]
    down = [(i + 1, i) for i in range(spaces - 1)]
    pieces = [slice(h * part, (h + 1) * part) for h in range(PARTS)]

    whole = jnp.transpose(dist, (1, 2, 0, 3)).reshape(rows, vb, nx)
    lo_all = lax.ppermute(whole[rows - ny :], "space", up)
    hi_all = lax.ppermute(whole[:ny], "space", down)
    fs = [whole[:, p] for p in pieces]
    for step in range(STEPS):
        recvs = []
        for h, p in enumerate(pieces):
            f = fs[h]
            if step == 0:
                lo, hi = lo_all[:, p], hi_all[:, p]
            else:
                lo = lax.ppermute(f[rows - ny :], "space", up)
                hi = lax.ppermute(f[:ny], "space", down)
            half = transport(f, lo, hi, coef[:, p], tm, ny)
            recvs.append(lax.all_to_all(half.reshape(groups, chunk, part, nx), "vel", 0, 0, tiled=True))
        moments = None
        for h, p in enumerate(pieces):
            term = jnp.einsum("ksv,srvx->krx", w3[:, :, p], recvs[h], preferred_element_type=jnp.float32)
            moments = term if moments is None else moments + term
        delta = (rates[:, None, None] * moments).astype(jnp.bfloat16)
        fs = []
        post = None
        for h, p in enumerate(pieces):
            recv = recvs[h]
            if post is not None:
                post, recv = lax.optimization_barrier((post, recv))
                fs[-1] = lax.all_to_all(post, "vel", 0, 0, tiled=True).reshape(rows, part, nx)
            adjustment = jnp.einsum("svk,krx->srvx", e3[:, p], delta, preferred_element_type=jnp.float32)
            post = (recv.astype(jnp.float32) - cm[None, :, None, :] * adjustment).astype(jnp.bfloat16)
            fs.append(None)
        fs[-1] = lax.all_to_all(post, "vel", 0, 0, tiled=True).reshape(rows, part, nx)
    whole = jnp.concatenate(fs, axis=1)
    return jnp.transpose(whole.reshape(nzl, ny, vb, nx), (2, 0, 1, 3))


def solution(mesh):
    placed = (P("vel", "space", None, None), P("vel"), P("space", None, None), P(), P(), P())
    return jax.shard_map(
        per_device,
        mesh=mesh,
        in_specs=placed,
        out_specs=P("vel", "space", None, None),
        check_vma=False,
    )
```

```python
import functools

import jax
import jax.numpy as jnp
from jax import lax
from jax.experimental import pallas as pl
from jax.experimental.pallas import tpu as pltpu
from jax.sharding import PartitionSpec as P


VGRID = 24
STEPS = 2
VBLOCK = 112
PARTS = 2


def components(vel_map):
    side = VGRID
    first = (vel_map // (side * side)).astype(jnp.float32)
    second = (vel_map // side % side).astype(jnp.float32)
    third = (vel_map % side).astype(jnp.float32)
    centre = (side - 1) / 2.0
    half_side = side / 2.0
    return (
        0.3 * (first - centre) / half_side,
        0.3 * (second - centre) / half_side,
        0.3 * (third - centre) / half_side,
    )


def transport_kernel(ny, f_ref, lo_ref, hi_ref, coef_ref, tm_ref, out_ref, ext_ref):
    rows, tv, nx = f_ref.shape
    ext_ref[pl.ds(0, ny)] = lo_ref[...].astype(jnp.float32)
    ext_ref[pl.ds(ny, rows)] = f_ref[...].astype(jnp.float32)
    ext_ref[pl.ds(ny + rows, ny)] = hi_ref[...].astype(jnp.float32)
    ax = coef_ref[0]
    ay = coef_ref[1]
    az = coef_ref[2]
    gx, gy, gz = ax > 0.0, ay > 0.0, az > 0.0
    wx, wy, wz = jnp.abs(ax), jnp.abs(ay), jnp.abs(az)
    lane = lax.broadcasted_iota(jnp.int32, (tv, nx), 1)
    edge_x = (gx & (lane == 0)) | (jnp.logical_not(gx) & (lane == nx - 1))
    zero = jnp.zeros((tv, nx), jnp.float32)

    for w in range(rows):
        y = w % ny
        e = w + ny
        c = ext_ref[e]
        n_x = jnp.where(edge_x, 0.0, jnp.where(gx, pltpu.roll(c, 1, 1), pltpu.roll(c, nx - 1, 1)))
        y_low = ext_ref[e - 1] if y > 0 else zero
        y_high = ext_ref[e + 1] if y < ny - 1 else zero
        n_y = jnp.where(gy, y_low, y_high)
        n_z = jnp.where(gz, ext_ref[e - ny], ext_ref[e + ny])
        flux = wx * (c - n_x) + wy * (c - n_y)
        flux = flux + wz * (c - n_z)
        out_ref[w] = (c - tm_ref[w : w + 1, :] * flux).astype(out_ref.dtype)


def transport(f, lo, hi, coef, tm, ny):
    rows, vb, nx = f.shape
    tv = min(VBLOCK, vb)
    return pl.pallas_call(
        functools.partial(transport_kernel, ny),
        out_shape=jax.ShapeDtypeStruct(f.shape, f.dtype),
        grid=(vb // tv,),
        in_specs=[
            pl.BlockSpec((rows, tv, nx), lambda i: (0, i, 0)),
            pl.BlockSpec((ny, tv, nx), lambda i: (0, i, 0)),
            pl.BlockSpec((ny, tv, nx), lambda i: (0, i, 0)),
            pl.BlockSpec((3, tv, nx), lambda i: (0, i, 0)),
            pl.BlockSpec((rows, nx), lambda i: (0, 0)),
        ],
        out_specs=pl.BlockSpec((rows, tv, nx), lambda i: (0, i, 0)),
        scratch_shapes=[pltpu.VMEM((rows + 2 * ny, tv, nx), jnp.float32)],
        cost_estimate=pl.CostEstimate(
            flops=20 * rows * vb * nx, transcendentals=0, bytes_accessed=4 * rows * vb * nx
        ),
    )(f, lo, hi, coef, tm)


def per_device(dist, vel_map, cell_mask, w_modes, e_modes, rates):
    vb, nzl, ny, nx = dist.shape
    rows = nzl * ny
    groups = lax.axis_size("vel")
    spaces = lax.axis_size("space")
    chunk = rows // groups
    kmodes = w_modes.shape[0]
    part = vb // PARTS
    comp_x, comp_y, comp_z = components(vel_map)
    coef = jnp.broadcast_to(jnp.stack([comp_x, comp_y, comp_z])[:, :, None], (3, vb, nx))
    tm = (cell_mask != 1).astype(jnp.float32).reshape(rows, nx)
    cmask = jnp.where(cell_mask == 0, 1.0, jnp.where(cell_mask == 2, 0.5, 0.0)).astype(jnp.float32)
    cm = lax.dynamic_slice_in_dim(cmask.reshape(rows, nx), lax.axis_index("vel") * chunk, chunk, 0)
    w3 = w_modes.reshape(kmodes, groups, vb)
    e3 = e_modes.reshape(groups, vb, kmodes)
    up = [(i, i + 1) for i in range(spaces - 1)]
    down = [(i + 1, i) for i in range(spaces - 1)]
    pieces = [slice(h * part, (h + 1) * part) for h in range(PARTS)]

    whole = jnp.transpose(dist, (1, 2, 0, 3)).reshape(rows, vb, nx)
    fs = [whole[:, p] for p in pieces]
    halos = []
    for f in fs:
        halos.append((lax.ppermute(f[rows - ny :], "space", up), lax.ppermute(f[:ny], "space", down)))
    for step in range(STEPS):
        recvs = []
        for h, p in enumerate(pieces):
            f = fs[h]
            if step == 0:
                lo, hi = halos[h]
            else:
                lo = lax.ppermute(f[rows - ny :], "space", up)
                hi = lax.ppermute(f[:ny], "space", down)
            half = transport(f, lo, hi, coef[:, p], tm, ny)
            recvs.append(lax.all_to_all(half.reshape(groups, chunk, part, nx), "vel", 0, 0, tiled=True))
        moments = None
        for h, p in enumerate(pieces):
            term = jnp.einsum("ksv,srvx->krx", w3[:, :, p], recvs[h], preferred_element_type=jnp.float32)
            moments = term if moments is None else moments + term
        delta = (rates[:, None, None] * moments).astype(jnp.bfloat16)
        fs = []
        post = None
        for h, p in enumerate(pieces):
            recv = recvs[h]
            if post is not None:
                post, recv = lax.optimization_barrier((post, recv))
                fs[-1] = lax.all_to_all(post, "vel", 0, 0, tiled=True).reshape(rows, part, nx)
            adjustment = jnp.einsum("svk,krx->srvx", e3[:, p], delta, preferred_element_type=jnp.float32)
            post = (recv.astype(jnp.float32) - cm[None, :, None, :] * adjustment).astype(jnp.bfloat16)
            fs.append(None)
        fs[-1] = lax.all_to_all(post, "vel", 0, 0, tiled=True).reshape(rows, part, nx)
    whole = jnp.concatenate(fs, axis=1)
    return jnp.transpose(whole.reshape(nzl, ny, vb, nx), (2, 0, 1, 3))


def solution(mesh):
    placed = (P("vel", "space", None, None), P("vel"), P("space", None, None), P(), P(), P())
    return jax.shard_map(
        per_device,
        mesh=mesh,
        in_specs=placed,
        out_specs=P("vel", "space", None, None),
        check_vma=False,
    )
```

```python
import functools

import jax
import jax.numpy as jnp
from jax import lax
from jax.experimental import pallas as pl
from jax.experimental.pallas import tpu as pltpu
from jax.sharding import PartitionSpec as P

VGRID = 24
STEPS = 2
VBLOCK = 112
PARTS = 2


def components(vel_map):
    side = VGRID
    first = (vel_map // (side * side)).astype(jnp.float32)
    second = (vel_map // side % side).astype(jnp.float32)
    third = (vel_map % side).astype(jnp.float32)
    centre = (side - 1) / 2.0
    half_side = side / 2.0
    return (
        0.3 * (first - centre) / half_side,
        0.3 * (second - centre) / half_side,
        0.3 * (third - centre) / half_side,
    )


def transport_kernel(ny, f_ref, lo_ref, hi_ref, coef_ref, tm_ref, out_ref, ext_ref):
    rows, tv, nx = f_ref.shape
    ext_ref[pl.ds(0, ny)] = lo_ref[...].astype(jnp.float32)
    ext_ref[pl.ds(ny, rows)] = f_ref[...].astype(jnp.float32)
    ext_ref[pl.ds(ny + rows, ny)] = hi_ref[...].astype(jnp.float32)
    ax = coef_ref[0]
    ay = coef_ref[1]
    az = coef_ref[2]
    gx, gy, gz = ax > 0.0, ay > 0.0, az > 0.0
    wx, wy, wz = jnp.abs(ax), jnp.abs(ay), jnp.abs(az)
    lane = lax.broadcasted_iota(jnp.int32, (tv, nx), 1)
    edge_x = (gx & (lane == 0)) | (jnp.logical_not(gx) & (lane == nx - 1))
    zero = jnp.zeros((tv, nx), jnp.float32)

    for w in range(rows):
        y = w % ny
        e = w + ny
        c = ext_ref[e]
        n_x = jnp.where(edge_x, 0.0, jnp.where(gx, pltpu.roll(c, 1, 1), pltpu.roll(c, nx - 1, 1)))
        y_low = ext_ref[e - 1] if y > 0 else zero
        y_high = ext_ref[e + 1] if y < ny - 1 else zero
        n_y = jnp.where(gy, y_low, y_high)
        n_z = jnp.where(gz, ext_ref[e - ny], ext_ref[e + ny])
        flux = wx * (c - n_x) + wy * (c - n_y)
        flux = flux + wz * (c - n_z)
        out_ref[w] = (c - tm_ref[w : w + 1, :] * flux).astype(out_ref.dtype)


def transport(f, lo, hi, coef, tm, ny):
    rows, vb, nx = f.shape
    tv = min(VBLOCK, vb)
    return pl.pallas_call(
        functools.partial(transport_kernel, ny),
        out_shape=jax.ShapeDtypeStruct(f.shape, f.dtype),
        grid=(vb // tv,),
        in_specs=[
            pl.BlockSpec((rows, tv, nx), lambda i: (0, i, 0)),
            pl.BlockSpec((ny, tv, nx), lambda i: (0, i, 0)),
            pl.BlockSpec((ny, tv, nx), lambda i: (0, i, 0)),
            pl.BlockSpec((3, tv, nx), lambda i: (0, i, 0)),
            pl.BlockSpec((rows, nx), lambda i: (0, 0)),
        ],
        out_specs=pl.BlockSpec((rows, tv, nx), lambda i: (0, i, 0)),
        scratch_shapes=[pltpu.VMEM((rows + 2 * ny, tv, nx), jnp.float32)],
        cost_estimate=pl.CostEstimate(
            flops=20 * rows * vb * nx, transcendentals=0, bytes_accessed=4 * rows * vb * nx
        ),
    )(f, lo, hi, coef, tm)


def per_device(dist, vel_map, cell_mask, w_modes, e_modes, rates):
    vb, nzl, ny, nx = dist.shape
    rows = nzl * ny
    groups = lax.axis_size("vel")
    spaces = lax.axis_size("space")
    chunk = rows // groups
    kmodes = w_modes.shape[0]
    part = vb // PARTS
    comp_x, comp_y, comp_z = components(vel_map)
    coef = jnp.broadcast_to(jnp.stack([comp_x, comp_y, comp_z])[:, :, None], (3, vb, nx))
    tm = (cell_mask != 1).astype(jnp.float32).reshape(rows, nx)
    cmask = jnp.where(cell_mask == 0, 1.0, jnp.where(cell_mask == 2, 0.5, 0.0)).astype(jnp.float32)
    cm = lax.dynamic_slice_in_dim(cmask.reshape(rows, nx), lax.axis_index("vel") * chunk, chunk, 0)
    w3 = w_modes.reshape(kmodes, groups, vb)
    e3 = e_modes.reshape(groups, vb, kmodes)
    up = [(i, i + 1) for i in range(spaces - 1)]
    down = [(i + 1, i) for i in range(spaces - 1)]
    pieces = [slice(h * part, (h + 1) * part) for h in range(PARTS)]

    whole = jnp.transpose(dist, (1, 2, 0, 3)).reshape(rows, vb, nx)
    lo = lax.ppermute(whole[rows - ny :], "space", up)
    hi = lax.ppermute(whole[:ny], "space", down)
    half = transport(whole, lo, hi, coef, tm, ny)
    recv = lax.all_to_all(half.reshape(groups, chunk, vb, nx), "vel", 0, 0, tiled=True)
    moments = jnp.einsum("ksv,srvx->krx", w3, recv, preferred_element_type=jnp.float32)
    delta = (rates[:, None, None] * moments).astype(jnp.bfloat16)
    fs = []
    for p in pieces:
        adjustment = jnp.einsum("svk,krx->srvx", e3[:, p], delta, preferred_element_type=jnp.float32)
        post = (recv[:, :, p].astype(jnp.float32) - cm[None, :, None, :] * adjustment).astype(jnp.bfloat16)
        fs.append(lax.all_to_all(post, "vel", 0, 0, tiled=True).reshape(rows, part, nx))
    recvs = []
    for h, p in enumerate(pieces):
        f = fs[h]
        lo = lax.ppermute(f[rows - ny :], "space", up)
        hi = lax.ppermute(f[:ny], "space", down)
        half = transport(f, lo, hi, coef[:, p], tm, ny)
        recvs.append(lax.all_to_all(half.reshape(groups, chunk, part, nx), "vel", 0, 0, tiled=True))
    moments = None
    for h, p in enumerate(pieces):
        term = jnp.einsum("ksv,srvx->krx", w3[:, :, p], recvs[h], preferred_element_type=jnp.float32)
        moments = term if moments is None else moments + term
    delta = (rates[:, None, None] * moments).astype(jnp.bfloat16)
    recv = jnp.concatenate(recvs, axis=2)
    adjustment = jnp.einsum("svk,krx->srvx", e3, delta, preferred_element_type=jnp.float32)
    post = (recv.astype(jnp.float32) - cm[None, :, None, :] * adjustment).astype(jnp.bfloat16)
    f = lax.all_to_all(post, "vel", 0, 0, tiled=True).reshape(rows, vb, nx)
    return jnp.transpose(f.reshape(nzl, ny, vb, nx), (2, 0, 1, 3))


def solution(mesh):
    placed = (P("vel", "space", None, None), P("vel"), P("space", None, None), P(), P(), P())
    return jax.shard_map(
        per_device,
        mesh=mesh,
        in_specs=placed,
        out_specs=P("vel", "space", None, None),
        check_vma=False,
    )
```

```python
import functools

import jax
import jax.numpy as jnp
from jax import lax
from jax.experimental import pallas as pl
from jax.experimental.pallas import tpu as pltpu
from jax.sharding import PartitionSpec as P

VGRID = 24
STEPS = 2
VBLOCK = 112
PARTS = 2


def components(vel_map):
    side = VGRID
    first = (vel_map // (side * side)).astype(jnp.float32)
    second = (vel_map // side % side).astype(jnp.float32)
    third = (vel_map % side).astype(jnp.float32)
    centre = (side - 1) / 2.0
    half_side = side / 2.0
    return (
        0.3 * (first - centre) / half_side,
        0.3 * (second - centre) / half_side,
        0.3 * (third - centre) / half_side,
    )


def transport_kernel(ny, f_ref, lo_ref, hi_ref, coef_ref, tm_ref, out_ref, ext_ref):
    rows, tv, nx = f_ref.shape
    ext_ref[pl.ds(0, ny)] = lo_ref[...].astype(jnp.float32)
    ext_ref[pl.ds(ny, rows)] = f_ref[...].astype(jnp.float32)
    ext_ref[pl.ds(ny + rows, ny)] = hi_ref[...].astype(jnp.float32)
    ax = coef_ref[0]
    ay = coef_ref[1]
    az = coef_ref[2]
    gx, gy, gz = ax > 0.0, ay > 0.0, az > 0.0
    wx, wy, wz = jnp.abs(ax), jnp.abs(ay), jnp.abs(az)
    lane = lax.broadcasted_iota(jnp.int32, (tv, nx), 1)
    edge_x = (gx & (lane == 0)) | (jnp.logical_not(gx) & (lane == nx - 1))
    zero = jnp.zeros((tv, nx), jnp.float32)

    for w in range(rows):
        y = w % ny
        e = w + ny
        c = ext_ref[e]
        n_x = jnp.where(edge_x, 0.0, jnp.where(gx, pltpu.roll(c, 1, 1), pltpu.roll(c, nx - 1, 1)))
        y_low = ext_ref[e - 1] if y > 0 else zero
        y_high = ext_ref[e + 1] if y < ny - 1 else zero
        n_y = jnp.where(gy, y_low, y_high)
        n_z = jnp.where(gz, ext_ref[e - ny], ext_ref[e + ny])
        flux = wx * (c - n_x) + wy * (c - n_y)
        flux = flux + wz * (c - n_z)
        out_ref[w] = (c - tm_ref[w : w + 1, :] * flux).astype(out_ref.dtype)


def transport(f, lo, hi, coef, tm, ny, part, first):
    rows, _, nx = f.shape
    tv = min(VBLOCK, part)
    base, cbase = first[0] * (part // tv), first[1] * (part // tv)
    return pl.pallas_call(
        functools.partial(transport_kernel, ny),
        out_shape=jax.ShapeDtypeStruct((rows, part, nx), f.dtype),
        grid=(part // tv,),
        in_specs=[
            pl.BlockSpec((rows, tv, nx), lambda i: (0, i + base, 0)),
            pl.BlockSpec((ny, tv, nx), lambda i: (0, i + base, 0)),
            pl.BlockSpec((ny, tv, nx), lambda i: (0, i + base, 0)),
            pl.BlockSpec((3, tv, nx), lambda i: (0, i + cbase, 0)),
            pl.BlockSpec((rows, nx), lambda i: (0, 0)),
        ],
        out_specs=pl.BlockSpec((rows, tv, nx), lambda i: (0, i, 0)),
        scratch_shapes=[pltpu.VMEM((rows + 2 * ny, tv, nx), jnp.float32)],
        cost_estimate=pl.CostEstimate(
            flops=20 * rows * part * nx, transcendentals=0, bytes_accessed=4 * rows * part * nx
        ),
    )(f, lo, hi, coef, tm)


def per_device(dist, vel_map, cell_mask, w_modes, e_modes, rates):
    vb, nzl, ny, nx = dist.shape
    rows = nzl * ny
    groups = lax.axis_size("vel")
    spaces = lax.axis_size("space")
    chunk = rows // groups
    kmodes = w_modes.shape[0]
    part = vb // PARTS
    comp_x, comp_y, comp_z = components(vel_map)
    coef = jnp.broadcast_to(jnp.stack([comp_x, comp_y, comp_z])[:, :, None], (3, vb, nx))
    tm = (cell_mask != 1).astype(jnp.float32).reshape(rows, nx)
    cmask = jnp.where(cell_mask == 0, 1.0, jnp.where(cell_mask == 2, 0.5, 0.0)).astype(jnp.float32)
    cm = lax.dynamic_slice_in_dim(cmask.reshape(rows, nx), lax.axis_index("vel") * chunk, chunk, 0)
    w3 = w_modes.reshape(kmodes, groups, vb)
    e3 = e_modes.reshape(groups, vb, kmodes)
    up = [(i, i + 1) for i in range(spaces - 1)]
    down = [(i + 1, i) for i in range(spaces - 1)]
    pieces = [slice(h * part, (h + 1) * part) for h in range(PARTS)]

    whole = jnp.transpose(dist, (1, 2, 0, 3)).reshape(rows, vb, nx)
    lo_all = lax.ppermute(whole[rows - ny :], "space", up)
    hi_all = lax.ppermute(whole[:ny], "space", down)
    fs = [whole] * PARTS
    for step in range(STEPS):
        recvs = []
        for h, p in enumerate(pieces):
            f = fs[h]
            if step == 0:
                lo, hi, first = lo_all, hi_all, (h, h)
            else:
                lo = lax.ppermute(f[rows - ny :], "space", up)
                hi = lax.ppermute(f[:ny], "space", down)
                first = (0, h)
            half = transport(f, lo, hi, coef, tm, ny, part, first)
            recvs.append(lax.all_to_all(half.reshape(groups, chunk, part, nx), "vel", 0, 0, tiled=True))
        moments = None
        for h, p in enumerate(pieces):
            term = jnp.einsum("ksv,srvx->krx", w3[:, :, p], recvs[h], preferred_element_type=jnp.float32)
            moments = term if moments is None else moments + term
        delta = (rates[:, None, None] * moments).astype(jnp.bfloat16)
        fs = []
        post = None
        for h, p in enumerate(pieces):
            recv = recvs[h]
            if post is not None:
                post, recv = lax.optimization_barrier((post, recv))
                fs[-1] = lax.all_to_all(post, "vel", 0, 0, tiled=True).reshape(rows, part, nx)
            adjustment = jnp.einsum("svk,krx->srvx", e3[:, p], delta, preferred_element_type=jnp.float32)
            post = (recv.astype(jnp.float32) - cm[None, :, None, :] * adjustment).astype(jnp.bfloat16)
            fs.append(None)
        fs[-1] = lax.all_to_all(post, "vel", 0, 0, tiled=True).reshape(rows, part, nx)
    whole = jnp.concatenate(fs, axis=1)
    return jnp.transpose(whole.reshape(nzl, ny, vb, nx), (2, 0, 1, 3))


def solution(mesh):
    placed = (P("vel", "space", None, None), P("vel"), P("space", None, None), P(), P(), P())
    return jax.shard_map(
        per_device,
        mesh=mesh,
        in_specs=placed,
        out_specs=P("vel", "space", None, None),
        check_vma=False,
    )
```

```python
import functools

import jax
import jax.numpy as jnp
from jax import lax
from jax.experimental import pallas as pl
from jax.experimental.pallas import tpu as pltpu
from jax.sharding import PartitionSpec as P

VGRID = 24
STEPS = 2
VBLOCK = 112
PARTS = 2


def components(vel_map):
    side = VGRID
    first = (vel_map // (side * side)).astype(jnp.float32)
    second = (vel_map // side % side).astype(jnp.float32)
    third = (vel_map % side).astype(jnp.float32)
    centre = (side - 1) / 2.0
    half_side = side / 2.0
    return (
        0.3 * (first - centre) / half_side,
        0.3 * (second - centre) / half_side,
        0.3 * (third - centre) / half_side,
    )


def transport_kernel(ny, f_ref, lo_ref, hi_ref, coef_ref, tm_ref, out_ref, ext_ref):
    rows, tv, nx = f_ref.shape
    ext_ref[pl.ds(0, ny)] = lo_ref[...].astype(jnp.float32)
    ext_ref[pl.ds(ny, rows)] = f_ref[...].astype(jnp.float32)
    ext_ref[pl.ds(ny + rows, ny)] = hi_ref[...].astype(jnp.float32)
    ax = coef_ref[0]
    ay = coef_ref[1]
    az = coef_ref[2]
    gx, gy, gz = ax > 0.0, ay > 0.0, az > 0.0
    wx, wy, wz = jnp.abs(ax), jnp.abs(ay), jnp.abs(az)
    lane = lax.broadcasted_iota(jnp.int32, (tv, nx), 1)
    edge_x = (gx & (lane == 0)) | (jnp.logical_not(gx) & (lane == nx - 1))
    zero = jnp.zeros((tv, nx), jnp.float32)

    for w in range(rows):
        y = w % ny
        e = w + ny
        c = ext_ref[e]
        n_x = jnp.where(edge_x, 0.0, jnp.where(gx, pltpu.roll(c, 1, 1), pltpu.roll(c, nx - 1, 1)))
        y_low = ext_ref[e - 1] if y > 0 else zero
        y_high = ext_ref[e + 1] if y < ny - 1 else zero
        n_y = jnp.where(gy, y_low, y_high)
        n_z = jnp.where(gz, ext_ref[e - ny], ext_ref[e + ny])
        flux = wx * (c - n_x) + wy * (c - n_y)
        flux = flux + wz * (c - n_z)
        out_ref[w] = (c - tm_ref[w : w + 1, :] * flux).astype(out_ref.dtype)


def transport(f, lo, hi, coef, tm, ny):
    rows, vb, nx = f.shape
    tv = min(VBLOCK, vb)
    return pl.pallas_call(
        functools.partial(transport_kernel, ny),
        out_shape=jax.ShapeDtypeStruct(f.shape, f.dtype),
        grid=(vb // tv,),
        in_specs=[
            pl.BlockSpec((rows, tv, nx), lambda i: (0, i, 0)),
            pl.BlockSpec((ny, tv, nx), lambda i: (0, i, 0)),
            pl.BlockSpec((ny, tv, nx), lambda i: (0, i, 0)),
            pl.BlockSpec((3, tv, nx), lambda i: (0, i, 0)),
            pl.BlockSpec((rows, nx), lambda i: (0, 0)),
        ],
        out_specs=pl.BlockSpec((rows, tv, nx), lambda i: (0, i, 0)),
        scratch_shapes=[pltpu.VMEM((rows + 2 * ny, tv, nx), jnp.float32)],
        cost_estimate=pl.CostEstimate(
            flops=20 * rows * vb * nx, transcendentals=0, bytes_accessed=4 * rows * vb * nx
        ),
    )(f, lo, hi, coef, tm)


def transpose_kernel(x_ref, o_ref):
    o_ref[...] = x_ref[...].astype(jnp.float32).T.astype(o_ref.dtype)


def transposed(w):
    rows, cols = w.shape
    tile = rows
    return pl.pallas_call(
        transpose_kernel,
        out_shape=jax.ShapeDtypeStruct((cols, rows), w.dtype),
        grid=(cols // tile,),
        in_specs=[pl.BlockSpec((rows, tile), lambda i: (0, i))],
        out_specs=pl.BlockSpec((tile, rows), lambda i: (i, 0)),
        cost_estimate=pl.CostEstimate(flops=0, transcendentals=0, bytes_accessed=4 * rows * cols),
    )(w)


def per_device(dist, vel_map, cell_mask, w_modes, e_modes, rates):
    vb, nzl, ny, nx = dist.shape
    rows = nzl * ny
    groups = lax.axis_size("vel")
    spaces = lax.axis_size("space")
    chunk = rows // groups
    kmodes = w_modes.shape[0]
    part = vb // PARTS
    comp_x, comp_y, comp_z = components(vel_map)
    coef = jnp.broadcast_to(jnp.stack([comp_x, comp_y, comp_z])[:, :, None], (3, vb, nx))
    tm = (cell_mask != 1).astype(jnp.float32).reshape(rows, nx)
    cmask = jnp.where(cell_mask == 0, 1.0, jnp.where(cell_mask == 2, 0.5, 0.0)).astype(jnp.float32)
    cm = lax.dynamic_slice_in_dim(cmask.reshape(rows, nx), lax.axis_index("vel") * chunk, chunk, 0)
    e3 = e_modes.reshape(groups, vb, kmodes)
    up = [(i, i + 1) for i in range(spaces - 1)]
    down = [(i + 1, i) for i in range(spaces - 1)]
    pieces = [slice(h * part, (h + 1) * part) for h in range(PARTS)]

    whole = jnp.transpose(dist, (1, 2, 0, 3)).reshape(rows, vb, nx)
    lo_all = lax.ppermute(whole[rows - ny :], "space", up)
    hi_all = lax.ppermute(whole[:ny], "space", down)
    wt, lo_all, hi_all = lax.optimization_barrier((transposed(w_modes), lo_all, hi_all))
    w3 = wt.reshape(groups, vb, kmodes)
    fs = [whole[:, p] for p in pieces]
    for step in range(STEPS):
        recvs = []
        for h, p in enumerate(pieces):
            f = fs[h]
            if step == 0:
                lo, hi = lo_all[:, p], hi_all[:, p]
            else:
                lo = lax.ppermute(f[rows - ny :], "space", up)
                hi = lax.ppermute(f[:ny], "space", down)
            half = transport(f, lo, hi, coef[:, p], tm, ny)
            recvs.append(lax.all_to_all(half.reshape(groups, chunk, part, nx), "vel", 0, 0, tiled=True))
        moments = None
        for h, p in enumerate(pieces):
            term = jnp.einsum("svk,srvx->krx", w3[:, p], recvs[h], preferred_element_type=jnp.float32)
            moments = term if moments is None else moments + term
        delta = (rates[:, None, None] * moments).astype(jnp.bfloat16)
        fs = []
        post = None
        for h, p in enumerate(pieces):
            recv = recvs[h]
            if post is not None:
                post, recv = lax.optimization_barrier((post, recv))
                fs[-1] = lax.all_to_all(post, "vel", 0, 0, tiled=True).reshape(rows, part, nx)
            adjustment = jnp.einsum("svk,krx->srvx", e3[:, p], delta, preferred_element_type=jnp.float32)
            post = (recv.astype(jnp.float32) - cm[None, :, None, :] * adjustment).astype(jnp.bfloat16)
            fs.append(None)
        fs[-1] = lax.all_to_all(post, "vel", 0, 0, tiled=True).reshape(rows, part, nx)
    whole = jnp.concatenate(fs, axis=1)
    return jnp.transpose(whole.reshape(nzl, ny, vb, nx), (2, 0, 1, 3))


def solution(mesh):
    placed = (P("vel", "space", None, None), P("vel"), P("space", None, None), P(), P(), P())
    return jax.shard_map(
        per_device,
        mesh=mesh,
        in_specs=placed,
        out_specs=P("vel", "space", None, None),
        check_vma=False,
    )
```

```python
import functools

import jax
import jax.numpy as jnp
from jax import lax
from jax.experimental import pallas as pl
from jax.experimental.pallas import tpu as pltpu
from jax.sharding import PartitionSpec as P

VGRID = 24
STEPS = 2
VBLOCK = 32
PARTS = 2


def components(vel_map):
    side = VGRID
    first = (vel_map // (side * side)).astype(jnp.float32)
    second = (vel_map // side % side).astype(jnp.float32)
    third = (vel_map % side).astype(jnp.float32)
    centre = (side - 1) / 2.0
    half_side = side / 2.0
    return (
        0.3 * (first - centre) / half_side,
        0.3 * (second - centre) / half_side,
        0.3 * (third - centre) / half_side,
    )


def transport_kernel(ny, f_ref, lo_ref, hi_ref, coef_ref, tm_ref, out_ref, ext_ref):
    rows, tv, nx = f_ref.shape
    ext_ref[pl.ds(0, ny)] = lo_ref[...].astype(jnp.float32)
    ext_ref[pl.ds(ny, rows)] = f_ref[...].astype(jnp.float32)
    ext_ref[pl.ds(ny + rows, ny)] = hi_ref[...].astype(jnp.float32)
    ax = coef_ref[0]
    ay = coef_ref[1]
    az = coef_ref[2]
    gx, gy, gz = ax > 0.0, ay > 0.0, az > 0.0
    wx, wy, wz = jnp.abs(ax), jnp.abs(ay), jnp.abs(az)
    lane = lax.broadcasted_iota(jnp.int32, (tv, nx), 1)
    edge_x = (gx & (lane == 0)) | (jnp.logical_not(gx) & (lane == nx - 1))
    zero = jnp.zeros((tv, nx), jnp.float32)

    for w in range(rows):
        y = w % ny
        e = w + ny
        c = ext_ref[e]
        n_x = jnp.where(edge_x, 0.0, jnp.where(gx, pltpu.roll(c, 1, 1), pltpu.roll(c, nx - 1, 1)))
        y_low = ext_ref[e - 1] if y > 0 else zero
        y_high = ext_ref[e + 1] if y < ny - 1 else zero
        n_y = jnp.where(gy, y_low, y_high)
        n_z = jnp.where(gz, ext_ref[e - ny], ext_ref[e + ny])
        flux = wx * (c - n_x) + wy * (c - n_y)
        flux = flux + wz * (c - n_z)
        out_ref[w] = (c - tm_ref[w : w + 1, :] * flux).astype(out_ref.dtype)


def transport(f, lo, hi, coef, tm, ny):
    rows, vb, nx = f.shape
    tv = min(VBLOCK, vb)
    return pl.pallas_call(
        functools.partial(transport_kernel, ny),
        out_shape=jax.ShapeDtypeStruct(f.shape, f.dtype),
        grid=(vb // tv,),
        in_specs=[
            pl.BlockSpec((rows, tv, nx), lambda i: (0, i, 0)),
            pl.BlockSpec((ny, tv, nx), lambda i: (0, i, 0)),
            pl.BlockSpec((ny, tv, nx), lambda i: (0, i, 0)),
            pl.BlockSpec((3, tv, nx), lambda i: (0, i, 0)),
            pl.BlockSpec((rows, nx), lambda i: (0, 0)),
        ],
        out_specs=pl.BlockSpec((rows, tv, nx), lambda i: (0, i, 0)),
        scratch_shapes=[pltpu.VMEM((rows + 2 * ny, tv, nx), jnp.float32)],
        cost_estimate=pl.CostEstimate(
            flops=20 * rows * vb * nx, transcendentals=0, bytes_accessed=4 * rows * vb * nx
        ),
    )(f, lo, hi, coef, tm)


def per_device(dist, vel_map, cell_mask, w_modes, e_modes, rates):
    vb, nzl, ny, nx = dist.shape
    rows = nzl * ny
    groups = lax.axis_size("vel")
    spaces = lax.axis_size("space")
    chunk = rows // groups
    kmodes = w_modes.shape[0]
    part = vb // PARTS
    comp_x, comp_y, comp_z = components(vel_map)
    coef = jnp.broadcast_to(jnp.stack([comp_x, comp_y, comp_z])[:, :, None], (3, vb, nx))
    tm = (cell_mask != 1).astype(jnp.float32).reshape(rows, nx)
    cmask = jnp.where(cell_mask == 0, 1.0, jnp.where(cell_mask == 2, 0.5, 0.0)).astype(jnp.float32)
    cm = lax.dynamic_slice_in_dim(cmask.reshape(rows, nx), lax.axis_index("vel") * chunk, chunk, 0)
    w3 = w_modes.reshape(kmodes, groups, vb)
    e3 = e_modes.reshape(groups, vb, kmodes)
    up = [(i, i + 1) for i in range(spaces - 1)]
    down = [(i + 1, i) for i in range(spaces - 1)]
    pieces = [slice(h * part, (h + 1) * part) for h in range(PARTS)]

    whole = jnp.transpose(dist, (1, 2, 0, 3)).reshape(rows, vb, nx)
    lo_all = lax.ppermute(whole[rows - ny :], "space", up)
    hi_all = lax.ppermute(whole[:ny], "space", down)
    fs = [whole[:, p] for p in pieces]
    for step in range(STEPS):
        recvs = []
        for h, p in enumerate(pieces):
            f = fs[h]
            if step == 0:
                lo, hi = lo_all[:, p], hi_all[:, p]
            else:
                lo = lax.ppermute(f[rows - ny :], "space", up)
                hi = lax.ppermute(f[:ny], "space", down)
            half = transport(f, lo, hi, coef[:, p], tm, ny)
            recvs.append(lax.all_to_all(half.reshape(groups, chunk, part, nx), "vel", 0, 0, tiled=True))
        moments = None
        for h, p in enumerate(pieces):
            term = jnp.einsum("ksv,srvx->krx", w3[:, :, p], recvs[h], preferred_element_type=jnp.float32)
            moments = term if moments is None else moments + term
        delta = (rates[:, None, None] * moments).astype(jnp.bfloat16)
        fs = []
        post = None
        for h, p in enumerate(pieces):
            recv = recvs[h]
            if post is not None:
                post, recv = lax.optimization_barrier((post, recv))
                fs[-1] = lax.all_to_all(post, "vel", 0, 0, tiled=True).reshape(rows, part, nx)
            adjustment = jnp.einsum("svk,krx->srvx", e3[:, p], delta, preferred_element_type=jnp.float32)
            post = (recv.astype(jnp.float32) - cm[None, :, None, :] * adjustment).astype(jnp.bfloat16)
            fs.append(None)
        fs[-1] = lax.all_to_all(post, "vel", 0, 0, tiled=True).reshape(rows, part, nx)
    whole = jnp.concatenate(fs, axis=1)
    return jnp.transpose(whole.reshape(nzl, ny, vb, nx), (2, 0, 1, 3))


def solution(mesh):
    placed = (P("vel", "space", None, None), P("vel"), P("space", None, None), P(), P(), P())
    return jax.shard_map(
        per_device,
        mesh=mesh,
        in_specs=placed,
        out_specs=P("vel", "space", None, None),
        check_vma=False,
    )
```

```python
import functools

import jax
import jax.numpy as jnp
from jax import lax
from jax.experimental import pallas as pl
from jax.experimental.pallas import tpu as pltpu
from jax.sharding import PartitionSpec as P

VGRID = 24
STEPS = 2
VBLOCK = 112
PARTS = 2


def components(vel_map):
    side = VGRID
    first = (vel_map // (side * side)).astype(jnp.float32)
    second = (vel_map // side % side).astype(jnp.float32)
    third = (vel_map % side).astype(jnp.float32)
    centre = (side - 1) / 2.0
    half_side = side / 2.0
    return (
        0.3 * (first - centre) / half_side,
        0.3 * (second - centre) / half_side,
        0.3 * (third - centre) / half_side,
    )


def transport_kernel(ny, f_ref, lo_ref, hi_ref, coef_ref, tm_ref, out_ref, ext_ref):
    rows, tv, nx = f_ref.shape
    ext_ref[pl.ds(0, ny)] = lo_ref[...].astype(jnp.float32)
    ext_ref[pl.ds(ny, rows)] = f_ref[...].astype(jnp.float32)
    ext_ref[pl.ds(ny + rows, ny)] = hi_ref[...].astype(jnp.float32)
    ax = coef_ref[0]
    ay = coef_ref[1]
    az = coef_ref[2]
    gx, gy, gz = ax > 0.0, ay > 0.0, az > 0.0
    wx, wy, wz = jnp.abs(ax), jnp.abs(ay), jnp.abs(az)
    lane = lax.broadcasted_iota(jnp.int32, (tv, nx), 1)
    edge_x = (gx & (lane == 0)) | (jnp.logical_not(gx) & (lane == nx - 1))
    zero = jnp.zeros((tv, nx), jnp.float32)

    for w in range(rows):
        y = w % ny
        e = w + ny
        c = ext_ref[e]
        n_x = jnp.where(edge_x, 0.0, jnp.where(gx, pltpu.roll(c, 1, 1), pltpu.roll(c, nx - 1, 1)))
        y_low = ext_ref[e - 1] if y > 0 else zero
        y_high = ext_ref[e + 1] if y < ny - 1 else zero
        n_y = jnp.where(gy, y_low, y_high)
        n_z = jnp.where(gz, ext_ref[e - ny], ext_ref[e + ny])
        flux = wx * (c - n_x) + wy * (c - n_y)
        flux = flux + wz * (c - n_z)
        out_ref[w] = (c - tm_ref[w : w + 1, :] * flux).astype(out_ref.dtype)


def transport(f, lo, hi, coef, tm, ny):
    rows, vb, nx = f.shape
    tv = min(VBLOCK, vb)
    return pl.pallas_call(
        functools.partial(transport_kernel, ny),
        out_shape=jax.ShapeDtypeStruct(f.shape, f.dtype),
        grid=(vb // tv,),
        in_specs=[
            pl.BlockSpec((rows, tv, nx), lambda i: (0, i, 0)),
            pl.BlockSpec((ny, tv, nx), lambda i: (0, i, 0)),
            pl.BlockSpec((ny, tv, nx), lambda i: (0, i, 0)),
            pl.BlockSpec((3, tv, nx), lambda i: (0, i, 0)),
            pl.BlockSpec((rows, nx), lambda i: (0, 0)),
        ],
        out_specs=pl.BlockSpec((rows, tv, nx), lambda i: (0, i, 0)),
        scratch_shapes=[pltpu.VMEM((rows + 2 * ny, tv, nx), jnp.float32)],
        cost_estimate=pl.CostEstimate(
            flops=20 * rows * vb * nx, transcendentals=0, bytes_accessed=4 * rows * vb * nx
        ),
    )(f, lo, hi, coef, tm)


def per_device(dist, vel_map, cell_mask, w_modes, e_modes, rates):
    vb, nzl, ny, nx = dist.shape
    rows = nzl * ny
    groups = lax.axis_size("vel")
    spaces = lax.axis_size("space")
    chunk = rows // groups
    kmodes = w_modes.shape[0]
    part = vb // PARTS
    comp_x, comp_y, comp_z = components(vel_map)
    coef = jnp.broadcast_to(jnp.stack([comp_x, comp_y, comp_z])[:, :, None], (3, vb, nx))
    tm = (cell_mask != 1).astype(jnp.float32).reshape(rows, nx)
    cmask = jnp.where(cell_mask == 0, 1.0, jnp.where(cell_mask == 2, 0.5, 0.0)).astype(jnp.float32)
    cm = lax.dynamic_slice_in_dim(cmask.reshape(rows, nx), lax.axis_index("vel") * chunk, chunk, 0)
    w3 = w_modes.reshape(kmodes, groups, vb)
    e3 = e_modes.reshape(groups, vb, kmodes)
    up = [(i, i + 1) for i in range(spaces - 1)]
    down = [(i + 1, i) for i in range(spaces - 1)]
    pieces = [slice(h * part, (h + 1) * part) for h in range(PARTS)]

    whole = jnp.transpose(dist, (1, 2, 0, 3)).reshape(rows, vb, nx)
    lo_all = jnp.transpose(lax.ppermute(dist[:, nzl - 1], "space", up), (1, 0, 2))
    hi_all = jnp.transpose(lax.ppermute(dist[:, 0], "space", down), (1, 0, 2))
    fs = [whole[:, p] for p in pieces]
    for step in range(STEPS):
        recvs = []
        for h, p in enumerate(pieces):
            f = fs[h]
            if step == 0:
                lo, hi = lo_all[:, p], hi_all[:, p]
            else:
                lo = lax.ppermute(f[rows - ny :], "space", up)
                hi = lax.ppermute(f[:ny], "space", down)
            half = transport(f, lo, hi, coef[:, p], tm, ny)
            recvs.append(lax.all_to_all(half.reshape(groups, chunk, part, nx), "vel", 0, 0, tiled=True))
        moments = None
        for h, p in enumerate(pieces):
            term = jnp.einsum("ksv,srvx->krx", w3[:, :, p], recvs[h], preferred_element_type=jnp.float32)
            moments = term if moments is None else moments + term
        delta = (rates[:, None, None] * moments).astype(jnp.bfloat16)
        fs = []
        post = None
        for h, p in enumerate(pieces):
            recv = recvs[h]
            if post is not None:
                post, recv = lax.optimization_barrier((post, recv))
                fs[-1] = lax.all_to_all(post, "vel", 0, 0, tiled=True).reshape(rows, part, nx)
            adjustment = jnp.einsum("svk,krx->srvx", e3[:, p], delta, preferred_element_type=jnp.float32)
            post = (recv.astype(jnp.float32) - cm[None, :, None, :] * adjustment).astype(jnp.bfloat16)
            fs.append(None)
        fs[-1] = lax.all_to_all(post, "vel", 0, 0, tiled=True).reshape(rows, part, nx)
    whole = jnp.concatenate(fs, axis=1)
    return jnp.transpose(whole.reshape(nzl, ny, vb, nx), (2, 0, 1, 3))


def solution(mesh):
    placed = (P("vel", "space", None, None), P("vel"), P("space", None, None), P(), P(), P())
    return jax.shard_map(
        per_device,
        mesh=mesh,
        in_specs=placed,
        out_specs=P("vel", "space", None, None),
        check_vma=False,
    )
```

```python
import functools

import jax
import jax.numpy as jnp
from jax import lax
from jax.experimental import pallas as pl
from jax.experimental.pallas import tpu as pltpu
from jax.sharding import PartitionSpec as P

VGRID = 24
STEPS = 2
VBLOCK = 112
PARTS = 2


def components(vel_map):
    side = VGRID
    first = (vel_map // (side * side)).astype(jnp.float32)
    second = (vel_map // side % side).astype(jnp.float32)
    third = (vel_map % side).astype(jnp.float32)
    centre = (side - 1) / 2.0
    half_side = side / 2.0
    return (
        0.3 * (first - centre) / half_side,
        0.3 * (second - centre) / half_side,
        0.3 * (third - centre) / half_side,
    )


def transport_kernel(ny, f_ref, lo_ref, hi_ref, coef_ref, tm_ref, out_ref, ext_ref):
    rows, tv, nx = f_ref.shape
    ext_ref[pl.ds(0, ny)] = lo_ref[...].astype(jnp.float32)
    ext_ref[pl.ds(ny, rows)] = f_ref[...].astype(jnp.float32)
    ext_ref[pl.ds(ny + rows, ny)] = hi_ref[...].astype(jnp.float32)
    ax = coef_ref[0]
    ay = coef_ref[1]
    az = coef_ref[2]
    gx, gy, gz = ax > 0.0, ay > 0.0, az > 0.0
    wx, wy, wz = jnp.abs(ax), jnp.abs(ay), jnp.abs(az)
    lane = lax.broadcasted_iota(jnp.int32, (tv, nx), 1)
    edge_x = (gx & (lane == 0)) | (jnp.logical_not(gx) & (lane == nx - 1))
    zero = jnp.zeros((tv, nx), jnp.float32)

    for w in range(rows):
        y = w % ny
        e = w + ny
        c = ext_ref[e]
        n_x = jnp.where(edge_x, 0.0, jnp.where(gx, pltpu.roll(c, 1, 1), pltpu.roll(c, nx - 1, 1)))
        y_low = ext_ref[e - 1] if y > 0 else zero
        y_high = ext_ref[e + 1] if y < ny - 1 else zero
        n_y = jnp.where(gy, y_low, y_high)
        n_z = jnp.where(gz, ext_ref[e - ny], ext_ref[e + ny])
        flux = wx * (c - n_x) + wy * (c - n_y)
        flux = flux + wz * (c - n_z)
        out_ref[w] = (c - tm_ref[w : w + 1, :] * flux).astype(out_ref.dtype)


def transport(f, lo, hi, coef, tm, ny):
    rows, vb, nx = f.shape
    tv = min(VBLOCK, vb)
    return pl.pallas_call(
        functools.partial(transport_kernel, ny),
        out_shape=jax.ShapeDtypeStruct(f.shape, f.dtype),
        grid=(vb // tv,),
        in_specs=[
            pl.BlockSpec((rows, tv, nx), lambda i: (0, i, 0)),
            pl.BlockSpec((ny, tv, nx), lambda i: (0, i, 0)),
            pl.BlockSpec((ny, tv, nx), lambda i: (0, i, 0)),
            pl.BlockSpec((3, tv, nx), lambda i: (0, i, 0)),
            pl.BlockSpec((rows, nx), lambda i: (0, 0)),
        ],
        out_specs=pl.BlockSpec((rows, tv, nx), lambda i: (0, i, 0)),
        scratch_shapes=[pltpu.VMEM((rows + 2 * ny, tv, nx), jnp.float32)],
        cost_estimate=pl.CostEstimate(
            flops=20 * rows * vb * nx, transcendentals=0, bytes_accessed=4 * rows * vb * nx
        ),
    )(f, lo, hi, coef, tm)


def per_device(dist, vel_map, cell_mask, w_modes, e_modes, rates):
    vb, nzl, ny, nx = dist.shape
    rows = nzl * ny
    groups = lax.axis_size("vel")
    spaces = lax.axis_size("space")
    chunk = rows // groups
    kmodes = w_modes.shape[0]
    part = vb // PARTS
    comp_x, comp_y, comp_z = components(vel_map)
    coef = jnp.broadcast_to(jnp.stack([comp_x, comp_y, comp_z])[:, :, None], (3, vb, nx))
    tm = (cell_mask != 1).astype(jnp.float32).reshape(rows, nx)
    cmask = jnp.where(cell_mask == 0, 1.0, jnp.where(cell_mask == 2, 0.5, 0.0)).astype(jnp.float32)
    cm = lax.dynamic_slice_in_dim(cmask.reshape(rows, nx), lax.axis_index("vel") * chunk, chunk, 0)
    w3 = w_modes.reshape(kmodes, groups, vb)
    e3 = e_modes.reshape(groups, vb, kmodes)
    up = [(i, i + 1) for i in range(spaces - 1)]
    down = [(i + 1, i) for i in range(spaces - 1)]
    pieces = [slice(h * part, (h + 1) * part) for h in range(PARTS)]

    whole = jnp.transpose(dist, (1, 2, 0, 3)).reshape(rows, vb, nx)
    lo_all = lax.ppermute(whole[rows - ny :], "space", up)
    hi_all = lax.ppermute(whole[:ny], "space", down)
    fs = [whole[:, p] for p in pieces]
    for step in range(STEPS):
        recvs = []
        for h, p in enumerate(pieces):
            f = fs[h]
            if step == 0:
                lo, hi = lo_all[:, p], hi_all[:, p]
            else:
                lo = lax.ppermute(f[rows - ny :], "space", up)
                hi = lax.ppermute(f[:ny], "space", down)
            half = transport(f, lo, hi, coef[:, p], tm, ny)
            recvs.append(lax.all_to_all(half.reshape(groups, chunk, part, nx), "vel", 0, 0, tiled=True))
        moments = None
        for h, p in enumerate(pieces):
            term = jnp.einsum("ksv,srvx->krx", w3[:, :, p], recvs[h], preferred_element_type=jnp.float32)
            moments = term if moments is None else moments + term
        delta = (rates[:, None, None] * moments).astype(jnp.bfloat16)
        fs = [None] * PARTS
        post = None
        last = None
        for h in (reversed(range(PARTS)) if step == 0 else range(PARTS)):
            p = pieces[h]
            recv = recvs[h]
            if post is not None:
                post, recv = lax.optimization_barrier((post, recv))
                fs[last] = lax.all_to_all(post, "vel", 0, 0, tiled=True).reshape(rows, part, nx)
            adjustment = jnp.einsum("svk,krx->srvx", e3[:, p], delta, preferred_element_type=jnp.float32)
            post = (recv.astype(jnp.float32) - cm[None, :, None, :] * adjustment).astype(jnp.bfloat16)
            last = h
        fs[last] = lax.all_to_all(post, "vel", 0, 0, tiled=True).reshape(rows, part, nx)
    whole = jnp.concatenate(fs, axis=1)
    return jnp.transpose(whole.reshape(nzl, ny, vb, nx), (2, 0, 1, 3))


def solution(mesh):
    placed = (P("vel", "space", None, None), P("vel"), P("space", None, None), P(), P(), P())
    return jax.shard_map(
        per_device,
        mesh=mesh,
        in_specs=placed,
        out_specs=P("vel", "space", None, None),
        check_vma=False,
    )
```

```python
import functools

import jax
import jax.numpy as jnp
from jax import lax
from jax.experimental import pallas as pl
from jax.experimental.pallas import tpu as pltpu
from jax.sharding import PartitionSpec as P

VGRID = 24
STEPS = 2
VBLOCK = 112
PARTS = 2


def components(vel_map):
    side = VGRID
    first = (vel_map // (side * side)).astype(jnp.float32)
    second = (vel_map // side % side).astype(jnp.float32)
    third = (vel_map % side).astype(jnp.float32)
    centre = (side - 1) / 2.0
    half_side = side / 2.0
    return (
        0.3 * (first - centre) / half_side,
        0.3 * (second - centre) / half_side,
        0.3 * (third - centre) / half_side,
    )


def transport_kernel(ny, f_ref, lo_ref, hi_ref, coef_ref, tm_ref, out_ref, ext_ref):
    rows, tv, nx = f_ref.shape
    ext_ref[pl.ds(0, ny)] = lo_ref[...].astype(jnp.float32)
    ext_ref[pl.ds(ny, rows)] = f_ref[...].astype(jnp.float32)
    ext_ref[pl.ds(ny + rows, ny)] = hi_ref[...].astype(jnp.float32)
    ax = coef_ref[0]
    ay = coef_ref[1]
    az = coef_ref[2]
    gx, gy, gz = ax > 0.0, ay > 0.0, az > 0.0
    wx, wy, wz = jnp.abs(ax), jnp.abs(ay), jnp.abs(az)
    lane = lax.broadcasted_iota(jnp.int32, (tv, nx), 1)
    edge_x = (gx & (lane == 0)) | (jnp.logical_not(gx) & (lane == nx - 1))
    zero = jnp.zeros((tv, nx), jnp.float32)

    for w in range(rows):
        y = w % ny
        e = w + ny
        c = ext_ref[e]
        n_x = jnp.where(edge_x, 0.0, jnp.where(gx, pltpu.roll(c, 1, 1), pltpu.roll(c, nx - 1, 1)))
        y_low = ext_ref[e - 1] if y > 0 else zero
        y_high = ext_ref[e + 1] if y < ny - 1 else zero
        n_y = jnp.where(gy, y_low, y_high)
        n_z = jnp.where(gz, ext_ref[e - ny], ext_ref[e + ny])
        flux = wx * (c - n_x) + wy * (c - n_y)
        flux = flux + wz * (c - n_z)
        out_ref[w] = (c - tm_ref[w : w + 1, :] * flux).astype(out_ref.dtype)


def transport(f, lo, hi, coef, tm, ny, halo_part=0):
    rows, vb, nx = f.shape
    tv = min(VBLOCK, vb)
    hb = halo_part * (vb // tv)
    return pl.pallas_call(
        functools.partial(transport_kernel, ny),
        out_shape=jax.ShapeDtypeStruct(f.shape, f.dtype),
        grid=(vb // tv,),
        in_specs=[
            pl.BlockSpec((rows, tv, nx), lambda i: (0, i, 0)),
            pl.BlockSpec((ny, tv, nx), lambda i: (0, i + hb, 0)),
            pl.BlockSpec((ny, tv, nx), lambda i: (0, i + hb, 0)),
            pl.BlockSpec((3, tv, nx), lambda i: (0, i, 0)),
            pl.BlockSpec((rows, nx), lambda i: (0, 0)),
        ],
        out_specs=pl.BlockSpec((rows, tv, nx), lambda i: (0, i, 0)),
        scratch_shapes=[pltpu.VMEM((rows + 2 * ny, tv, nx), jnp.float32)],
        cost_estimate=pl.CostEstimate(
            flops=20 * rows * vb * nx, transcendentals=0, bytes_accessed=4 * rows * vb * nx
        ),
    )(f, lo, hi, coef, tm)


def per_device(dist, vel_map, cell_mask, w_modes, e_modes, rates):
    vb, nzl, ny, nx = dist.shape
    rows = nzl * ny
    groups = lax.axis_size("vel")
    spaces = lax.axis_size("space")
    chunk = rows // groups
    kmodes = w_modes.shape[0]
    part = vb // PARTS
    comp_x, comp_y, comp_z = components(vel_map)
    coef = jnp.broadcast_to(jnp.stack([comp_x, comp_y, comp_z])[:, :, None], (3, vb, nx))
    tm = (cell_mask != 1).astype(jnp.float32).reshape(rows, nx)
    cmask = jnp.where(cell_mask == 0, 1.0, jnp.where(cell_mask == 2, 0.5, 0.0)).astype(jnp.float32)
    cm = lax.dynamic_slice_in_dim(cmask.reshape(rows, nx), lax.axis_index("vel") * chunk, chunk, 0)
    w3 = w_modes.reshape(kmodes, groups, vb)
    e3 = e_modes.reshape(groups, vb, kmodes)
    up = [(i, i + 1) for i in range(spaces - 1)]
    down = [(i + 1, i) for i in range(spaces - 1)]
    pieces = [slice(h * part, (h + 1) * part) for h in range(PARTS)]

    whole = jnp.transpose(dist, (1, 2, 0, 3)).reshape(rows, vb, nx)
    lo_all = lax.ppermute(whole[rows - ny :], "space", up)
    hi_all = lax.ppermute(whole[:ny], "space", down)
    fs = [whole[:, p] for p in pieces]
    for step in range(STEPS):
        recvs = []
        for h, p in enumerate(pieces):
            f = fs[h]
            if step == 0:
                lo, hi, hp = lo_all, hi_all, h
            else:
                lo = lax.ppermute(f[rows - ny :], "space", up)
                hi = lax.ppermute(f[:ny], "space", down)
                hp = 0
            half = transport(f, lo, hi, coef[:, p], tm, ny, hp)
            recvs.append(lax.all_to_all(half.reshape(groups, chunk, part, nx), "vel", 0, 0, tiled=True))
        moments = None
        for h, p in enumerate(pieces):
            term = jnp.einsum("ksv,srvx->krx", w3[:, :, p], recvs[h], preferred_element_type=jnp.float32)
            moments = term if moments is None else moments + term
        delta = (rates[:, None, None] * moments).astype(jnp.bfloat16)
        fs = []
        post = None
        for h, p in enumerate(pieces):
            recv = recvs[h]
            if post is not None:
                post, recv = lax.optimization_barrier((post, recv))
                fs[-1] = lax.all_to_all(post, "vel", 0, 0, tiled=True).reshape(rows, part, nx)
            adjustment = jnp.einsum("svk,krx->srvx", e3[:, p], delta, preferred_element_type=jnp.float32)
            post = (recv.astype(jnp.float32) - cm[None, :, None, :] * adjustment).astype(jnp.bfloat16)
            fs.append(None)
        fs[-1] = lax.all_to_all(post, "vel", 0, 0, tiled=True).reshape(rows, part, nx)
    whole = jnp.concatenate(fs, axis=1)
    return jnp.transpose(whole.reshape(nzl, ny, vb, nx), (2, 0, 1, 3))


def solution(mesh):
    placed = (P("vel", "space", None, None), P("vel"), P("space", None, None), P(), P(), P())
    return jax.shard_map(
        per_device,
        mesh=mesh,
        in_specs=placed,
        out_specs=P("vel", "space", None, None),
        check_vma=False,
    )
```
